512 devices in a mesh: ind: 16 (over z, core), blk: 32 (over x, y).
Axes of the slice: x: 4, y: 8, z: 8, core: 2. Of those that a mesh axis runs over, the one named last changes fastest.
Arguments:
- genotypes: int32 [1024, 65536], P('ind', 'blk'), may hold values from 0 to 2, as said below
- block_units: int32 [64], replicated, may hold values from 4 to 32, as said below
- sketch_seed: int32 [1], replicated, may hold values from 0 to 999999
Outputs:
- basis: float32 [65536, 256], P(('blk', 'ind'))
The draws below stay inside these ranges and needn't reach their ends.
Inputs may be any that keep to these rules, and one draw needn't show every extreme that they name: `block_units`: every block holds between 4 and 32 units; the units of all blocks sum to 512; one block holds exactly 32 and some hold exactly 4. `genotypes`: dosages are 0, 1 or 2.
All inputs are finite; a program needn't handle non-finite values.
Results may differ from the reference program's by a relative error of at most 0.0041.
Values sent between devices are 32-bit elements; how exact they have to be, the bound alone decides.
No kernel may reach another device: no remote copies, remote signals or barrier semaphores. Data moves between devices by JAX's collectives and lax.ppermute only.
A program may use at most 64 MiB of HBM per device.

```python
import jax
import jax.numpy as jnp
from jax import lax

K = 256
UNIT = 128
NIND = 1024
NSNP = 65536
NBLK = 64


def draw_genotypes(key, part):
    subkeys = jax.random.split(key, 2)
    permille = jax.random.randint(subkeys[0], (1, NSNP), 50, 501)
    paired = jax.random.randint(subkeys[1], (NIND, NSNP), 0, 1000000)
    first_allele = (paired // 1000 < permille).astype(jnp.int32)
    second_allele = (paired % 1000 < permille).astype(jnp.int32)
    return first_allele + second_allele


def draw_block_units(key, part):
    subkeys = jax.random.split(key, 2)
    others = NBLK - 6
    extra_total = 4 * NBLK - 48
    profile = [entry_id * 2 * extra_total // (others * others) for entry_id in range(others)]
    remaining = extra_total - sum(profile)
    position = others - 1
    while remaining > 0:
        profile[position] = profile[position] + 1
        remaining = remaining - 1
        position = position - 1 if position > 1 else others - 1
    size_pool = jnp.array([32] + [4 + step_units for step_units in profile], dtype=jnp.int32)
    pool_count = NBLK - 5
    shuffled = size_pool[jax.random.permutation(subkeys[0], pool_count)]
    cut_at = jax.random.randint(subkeys[1], (), 0, pool_count + 1)
    pool_ids = jnp.arange(pool_count, dtype=jnp.int32)
    prefix_sum = jnp.sum(jnp.where(pool_ids < cut_at, shuffled, 0))
    adjuster = 4 + jnp.mod(-3 - prefix_sum, 16)
    final_units = 28 - adjuster
    places = jnp.arange(NBLK, dtype=jnp.int32)
    from_pool = jnp.where(places < cut_at, places, places - 4)
    from_pool = jnp.clip(from_pool, 0, pool_count - 1)
    block_sizes = shuffled[from_pool]
    block_sizes = jnp.where(places == cut_at, adjuster, block_sizes)
    block_sizes = jnp.where(jnp.logical_and(places > cut_at, places <= cut_at + 3), 4, block_sizes)
    block_sizes = jnp.where(places == NBLK - 1, final_units, block_sizes)
    return block_sizes.astype(jnp.int32)


def setup_inputs(seed: int = 0) -> dict:
    seeds = jax.random.split(jax.random.key(seed), 4)
    genotypes = draw_genotypes(jax.random.fold_in(seeds[3], 71), 0)
    block_units = draw_block_units(jax.random.fold_in(seeds[3], 71), 0)
    sketch_seed = jax.random.randint(seeds[2], (1,), 0, 1000000).astype(jnp.int32)
    return {"genotypes": genotypes, "block_units": block_units, "sketch_seed": sketch_seed}


SHRINKAGE = 0.25

def sketch_signs(columns, seed_value, lane_count):
    lane_ids = jnp.arange(lane_count, dtype=jnp.int32)
    hashed = columns[:, None] * lane_count + lane_ids[None, :]
    hashed = jnp.bitwise_xor(hashed, seed_value)
    hashed = hashed * 73244475
    hashed = jnp.bitwise_xor(hashed, jnp.right_shift(hashed, 16))
    hashed = hashed * 73244475
    hashed = jnp.bitwise_xor(hashed, jnp.right_shift(hashed, 16))
    parity = jnp.bitwise_and(jnp.right_shift(hashed, 5), 1)
    return (1 - 2 * parity).astype(jnp.float32)

def reference(genotypes, block_units, sketch_seed):
    dosage = genotypes.astype(jnp.float32)
    people = dosage.shape[0]
    average = lax.optimization_barrier(jnp.sum(dosage, 0)) / people
    spread_sq = lax.optimization_barrier(jnp.sum(dosage * dosage, 0)) / people - average * average
    standard = ((dosage - average) * lax.rsqrt(spread_sq + 1e-05)).astype(jnp.bfloat16)
    widths = block_units * UNIT
    block_ends = jnp.cumsum(widths, dtype=jnp.int32)
    block_starts = block_ends - widths
    tile_count = NSNP // UNIT
    tile_start = jnp.arange(tile_count, dtype=jnp.int32) * UNIT
    tile_block = lax.optimization_barrier(jnp.sum((tile_start[:, None] >= block_starts[None, :]).astype(jnp.int32), axis=1)).astype(jnp.int32) - 1
    seed_value = sketch_seed[0]

    def sketch_tile(running, tile_id):
        columns = tile_id * UNIT + jnp.arange(UNIT, dtype=jnp.int32)
        pieces = lax.dynamic_slice_in_dim(standard, tile_id * UNIT, UNIT, 1)
        sign_rows = sketch_signs(columns, seed_value, K).astype(jnp.bfloat16)
        block_id = tile_block[tile_id]
        return (running.at[block_id].add(jnp.dot(pieces.astype(jnp.float32), sign_rows.astype(jnp.float32), preferred_element_type=jnp.float32)), None)
    block_sums, _ = lax.scan(sketch_tile, jnp.zeros((NBLK, people, K), jnp.float32), jnp.arange(tile_count, dtype=jnp.int32))
    sketch = block_sums.astype(jnp.bfloat16)

    def rows_tile(gram_sums, tile_id):
        columns = tile_id * UNIT + jnp.arange(UNIT, dtype=jnp.int32)
        pieces = lax.dynamic_slice_in_dim(standard, tile_id * UNIT, UNIT, 1)
        sign_rows = sketch_signs(columns, seed_value, K)
        block_id = tile_block[tile_id]
        product = lax.dot_general(pieces.astype(jnp.float32), sketch[block_id].astype(jnp.float32), (((0,), (0,)), ((), ())), preferred_element_type=jnp.float32)
        projected = product * ((1.0 - SHRINKAGE) / people) + SHRINKAGE * sign_rows
        outer = lax.dot_general(projected.astype(jnp.float32), projected.astype(jnp.float32), (((0,), (0,)), ((), ())), precision=lax.Precision.HIGHEST, preferred_element_type=jnp.float32)
        return (gram_sums.at[block_id].add(outer), projected)
    gram_sums, projected_tiles = lax.scan(rows_tile, jnp.zeros((NBLK, K, K), jnp.float32), jnp.arange(tile_count, dtype=jnp.int32))
    gram_sums = gram_sums / widths.astype(jnp.float32)[:, None, None]
    factor = jnp.linalg.cholesky(gram_sums)

    def solve_tile(projected, block_id):
        return jax.scipy.linalg.solve_triangular(factor[block_id], projected.T, lower=True).T
    basis_rows = jax.vmap(solve_tile)(projected_tiles, tile_block)
    return basis_rows.reshape(NSNP, K)
```

```python
import math

import jax
import jax.numpy as jnp
from jax import lax
from jax.sharding import PartitionSpec as P

K = 256
UNIT = 128
MAX_UNITS = 32
MIN_UNITS = 4

SHRINKAGE = 0.25


def sketch_signs(columns, seed_value, lane_count):
    lane_ids = jnp.arange(lane_count, dtype=jnp.int32)
    hashed = columns[:, None] * lane_count + lane_ids[None, :]
    hashed = jnp.bitwise_xor(hashed, seed_value)
    hashed = hashed * 73244475
    hashed = jnp.bitwise_xor(hashed, jnp.right_shift(hashed, 16))
    hashed = hashed * 73244475
    hashed = jnp.bitwise_xor(hashed, jnp.right_shift(hashed, 16))
    parity = jnp.bitwise_and(jnp.right_shift(hashed, 5), 1)
    return (1 - 2 * parity).astype(jnp.float32)


def xor_allreduce(x, axis, count):
    mask = 1
    while mask < count:
        x = x + lax.ppermute(x, axis, [(j, j ^ mask) for j in range(count)])
        mask *= 2
    return x


def halving_allreduce(x, axis, count):
    place = lax.axis_index(axis)
    masks = []
    mask = 1
    while mask < count:
        masks.append(mask)
        mask *= 2
    for mask in masks:
        half = x.shape[0] // 2
        lower, upper = x[:half], x[half:]
        high = (place & mask) != 0
        send = jnp.where(high, lower, upper)
        keep = jnp.where(high, upper, lower)
        x = keep + lax.ppermute(send, axis, [(j, j ^ mask) for j in range(count)])
    for mask in reversed(masks):
        got = lax.ppermute(x, axis, [(j, j ^ mask) for j in range(count)])
        high = (place & mask) != 0
        x = jnp.where(high, jnp.concatenate([got, x], 0), jnp.concatenate([x, got], 0))
    return x


def shift(x, axis, count, step):
    pairs = [(j, j + step) for j in range(count) if 0 <= j + step < count]
    return lax.ppermute(x, axis, pairs)


def block_of(col, block_starts):
    return jnp.sum((col[..., None] >= block_starts).astype(jnp.int32), axis=-1) - 1


def halo(head_part, tail_part, blk_index, blk_count, reach, edge_blocks, first_block, last_block):
    from_lower = []
    from_upper = []
    for step in range(1, reach + 1):
        got_tail = shift(tail_part, "blk", blk_count, step)
        got_head = shift(head_part, "blk", blk_count, -step)
        lower = blk_index - step
        upper = blk_index + step
        lower_ok = jnp.logical_and(
            lower >= 0, edge_blocks[jnp.clip(lower, 0, blk_count - 1), 1] == first_block
        )
        upper_ok = jnp.logical_and(
            upper < blk_count, edge_blocks[jnp.clip(upper, 0, blk_count - 1), 0] == last_block
        )
        from_lower.append(jnp.where(lower_ok, got_tail, 0.0))
        from_upper.append(jnp.where(upper_ok, got_head, 0.0))
    return sum(from_lower[1:], from_lower[0]), sum(from_upper[1:], from_upper[0])


def on_device(genotypes, block_units, sketch_seed):
    ind_count = lax.axis_size("ind")
    blk_count = lax.axis_size("blk")
    people, col_span = genotypes.shape
    everyone = people * ind_count
    row_slice = col_span // ind_count
    unit_count = col_span // UNIT
    slot_total = (unit_count - 1) // MIN_UNITS + 2
    reach = min(-(-(MAX_UNITS - 1) // unit_count), blk_count - 1)
    blk_index = lax.axis_index("blk")
    ind_index = lax.axis_index("ind")

    dosage = genotypes.astype(jnp.float32)
    stats = xor_allreduce(jnp.stack([jnp.sum(dosage, 0), jnp.sum(dosage * dosage, 0)]), "ind", ind_count)
    average = stats[0] / everyone
    spread_sq = stats[1] / everyone - average * average
    standard = ((dosage - average) * lax.rsqrt(spread_sq + 1e-05)).astype(jnp.bfloat16)

    widths = block_units * UNIT
    block_ends = jnp.cumsum(widths, dtype=jnp.int32)
    block_starts = block_ends - widths
    col_base = blk_index * col_span
    unit_cols = col_base + jnp.arange(unit_count, dtype=jnp.int32) * UNIT
    unit_block = block_of(unit_cols, block_starts)
    first_block = unit_block[0]
    last_block = unit_block[unit_count - 1]
    unit_slot = unit_block - first_block
    group_bases = jnp.arange(blk_count, dtype=jnp.int32) * col_span
    edge_blocks = jnp.stack(
        [block_of(group_bases, block_starts), block_of(group_bases + col_span - 1, block_starts)], 1
    )
    last_slot = last_block - first_block

    columns = col_base + jnp.arange(col_span, dtype=jnp.int32)
    signs = sketch_signs(columns, sketch_seed[0], K)
    slot_ids = jnp.arange(slot_total, dtype=jnp.int32)
    col_slot = jnp.repeat(unit_slot, UNIT)
    col_mask = col_slot[None, :] == slot_ids[:, None]
    masked_std = jnp.where(col_mask[:, None, :], standard[None], jnp.zeros((), jnp.bfloat16))

    parts = jnp.einsum(
        "snc,ck->snk", masked_std, signs.astype(jnp.bfloat16), preferred_element_type=jnp.float32
    )
    head_in, tail_in = halo(
        parts[0], parts[last_slot], blk_index, blk_count, reach, edge_blocks, first_block, last_block
    )
    parts = parts.at[0].add(head_in)
    parts = parts.at[last_slot].add(tail_in)
    sketch = parts.astype(jnp.bfloat16)

    product = jnp.einsum("snc,snk->ck", masked_std, sketch, preferred_element_type=jnp.float32)
    product = halving_allreduce(product, "ind", ind_count)
    projected = product * ((1.0 - SHRINKAGE) / everyone) + SHRINKAGE * signs

    row_start = ind_index * row_slice
    my_rows = lax.dynamic_slice_in_dim(projected, row_start, row_slice, 0)
    my_slot = unit_slot[row_start // UNIT]
    pick = jnp.stack([col_slot == 0, col_slot == last_slot, col_slot == my_slot]).astype(jnp.float32)
    grams = jnp.einsum(
        "mc,ck,cl->mkl",
        pick,
        projected,
        projected,
        precision=lax.Precision.HIGHEST,
        preferred_element_type=jnp.float32,
    )
    head_in, tail_in = halo(
        grams[0], grams[1], blk_index, blk_count, reach, edge_blocks, first_block, last_block
    )
    gram = grams[2]
    gram = gram + jnp.where(my_slot == 0, head_in, 0.0)
    gram = gram + jnp.where(my_slot == last_slot, tail_in, 0.0)
    my_block = first_block + my_slot
    gram = gram / (block_units[my_block] * UNIT).astype(jnp.float32)
    factor = jnp.linalg.cholesky(gram)
    return jax.scipy.linalg.solve_triangular(factor, my_rows.T, lower=True).T


def solution(mesh):
    return jax.shard_map(
        on_device,
        mesh=mesh,
        in_specs=(P("ind", "blk"), P(), P()),
        out_specs=P(("blk", "ind"), None),
        check_vma=False,
    )
```

```python
import math

import jax
import jax.numpy as jnp
from jax import lax
from jax.sharding import PartitionSpec as P

K = 256
UNIT = 128
MAX_UNITS = 32
MIN_UNITS = 4

SHRINKAGE = 0.25


def sketch_signs(columns, seed_value, lane_count):
    lane_ids = jnp.arange(lane_count, dtype=jnp.int32)
    hashed = columns[:, None] * lane_count + lane_ids[None, :]
    hashed = jnp.bitwise_xor(hashed, seed_value)
    hashed = hashed * 73244475
    hashed = jnp.bitwise_xor(hashed, jnp.right_shift(hashed, 16))
    hashed = hashed * 73244475
    hashed = jnp.bitwise_xor(hashed, jnp.right_shift(hashed, 16))
    parity = jnp.bitwise_and(jnp.right_shift(hashed, 5), 1)
    return (1 - 2 * parity).astype(jnp.float32)


def digit_rounds(count):
    rounds = []
    bit = 0
    while (1 << bit) < count:
        radix = 4 if (4 << bit) <= count else 2
        rounds.append((bit, radix))
        bit += 2 if radix == 4 else 1
    return rounds


def exact_allreduce(x, axis, count):
    for bit, radix in digit_rounds(count):
        got = [
            lax.ppermute(x, axis, [(j, j ^ (o << bit)) for j in range(count)])
            for o in range(1, radix)
        ]
        x = x + sum(got[1:], got[0])
    return x


def chunked_allreduce(x, axis, count):
    place = lax.axis_index(axis)
    rounds = digit_rounds(count)
    for bit, radix in rounds:
        digit = (place >> bit) & (radix - 1)
        piece = x.shape[0] // radix
        parts = [lax.dynamic_slice_in_dim(x, (digit ^ o) * piece, piece, 0) for o in range(radix)]
        total = parts[0]
        for o in range(1, radix):
            total = total + lax.ppermute(
                parts[o], axis, [(j, j ^ (o << bit)) for j in range(count)]
            )
        x = total
    for bit, radix in reversed(rounds):
        digit = (place >> bit) & (radix - 1)
        got = [x] + [
            lax.ppermute(x, axis, [(j, j ^ (o << bit)) for j in range(count)])
            for o in range(1, radix)
        ]
        pieces = []
        for t in range(radix):
            offset = t ^ digit
            pick = got[radix - 1]
            for o in range(radix - 2, -1, -1):
                pick = jnp.where(offset == o, got[o], pick)
            pieces.append(pick)
        x = jnp.concatenate(pieces, 0)
    return x


def dot_hi(a, b):
    return jnp.dot(a, b, precision=lax.Precision.HIGHEST, preferred_element_type=jnp.float32)


def lower_inverse(lower):
    eye = jnp.eye(lower.shape[0], dtype=lower.dtype)
    return jax.scipy.linalg.solve_triangular(lower, eye, lower=True)


def basis_rows(gram, rows):
    half = gram.shape[0] // 2
    l11 = jnp.linalg.cholesky(gram[:half, :half])
    m11 = lower_inverse(l11)
    l21 = dot_hi(gram[half:, :half], m11.T)
    l22 = jnp.linalg.cholesky(gram[half:, half:] - dot_hi(l21, l21.T))
    m22 = lower_inverse(l22)
    m21 = -dot_hi(m22, dot_hi(l21, m11))
    left = dot_hi(rows[:, :half], m11.T)
    right = dot_hi(rows[:, :half], m21.T) + dot_hi(rows[:, half:], m22.T)
    return jnp.concatenate([left, right], 1)


def shift(x, axis, count, step):
    pairs = [(j, j + step) for j in range(count) if 0 <= j + step < count]
    return lax.ppermute(x, axis, pairs)


def block_of(col, block_starts):
    return jnp.sum((col[..., None] >= block_starts).astype(jnp.int32), axis=-1) - 1


def halo(head_part, tail_part, blk_index, blk_count, reach, edge_blocks, first_block, last_block):
    from_lower = []
    from_upper = []
    for step in range(1, reach + 1):
        got_tail = shift(tail_part, "blk", blk_count, step)
        got_head = shift(head_part, "blk", blk_count, -step)
        lower = blk_index - step
        upper = blk_index + step
        lower_ok = jnp.logical_and(
            lower >= 0, edge_blocks[jnp.clip(lower, 0, blk_count - 1), 1] == first_block
        )
        upper_ok = jnp.logical_and(
            upper < blk_count, edge_blocks[jnp.clip(upper, 0, blk_count - 1), 0] == last_block
        )
        from_lower.append(jnp.where(lower_ok, got_tail, 0.0))
        from_upper.append(jnp.where(upper_ok, got_head, 0.0))
    return sum(from_lower[1:], from_lower[0]), sum(from_upper[1:], from_upper[0])


def on_device(genotypes, block_units, sketch_seed):
    ind_count = lax.axis_size("ind")
    blk_count = lax.axis_size("blk")
    people, col_span = genotypes.shape
    everyone = people * ind_count
    row_slice = col_span // ind_count
    unit_count = col_span // UNIT
    slot_total = (unit_count - 1) // MIN_UNITS + 2
    reach = min(-(-(MAX_UNITS - 1) // unit_count), blk_count - 1)
    blk_index = lax.axis_index("blk")
    ind_index = lax.axis_index("ind")

    dosage = genotypes.astype(jnp.float32)
    stats = exact_allreduce(jnp.stack([jnp.sum(dosage, 0), jnp.sum(dosage * dosage, 0)]), "ind", ind_count)
    average = stats[0] / everyone
    spread_sq = stats[1] / everyone - average * average
    standard = ((dosage - average) * lax.rsqrt(spread_sq + 1e-05)).astype(jnp.bfloat16)

    widths = block_units * UNIT
    block_ends = jnp.cumsum(widths, dtype=jnp.int32)
    block_starts = block_ends - widths
    col_base = blk_index * col_span
    unit_cols = col_base + jnp.arange(unit_count, dtype=jnp.int32) * UNIT
    unit_block = block_of(unit_cols, block_starts)
    first_block = unit_block[0]
    last_block = unit_block[unit_count - 1]
    unit_slot = unit_block - first_block
    group_bases = jnp.arange(blk_count, dtype=jnp.int32) * col_span
    edge_blocks = jnp.stack(
        [block_of(group_bases, block_starts), block_of(group_bases + col_span - 1, block_starts)], 1
    )
    last_slot = last_block - first_block

    columns = col_base + jnp.arange(col_span, dtype=jnp.int32)
    signs = sketch_signs(columns, sketch_seed[0], K)
    slot_ids = jnp.arange(slot_total, dtype=jnp.int32)
    col_slot = jnp.repeat(unit_slot, UNIT)
    col_mask = col_slot[None, :] == slot_ids[:, None]
    masked_std = jnp.where(col_mask[:, None, :], standard[None], jnp.zeros((), jnp.bfloat16))

    parts = jnp.einsum(
        "snc,ck->snk", masked_std, signs.astype(jnp.bfloat16), preferred_element_type=jnp.float32
    )
    head_in, tail_in = halo(
        parts[0], parts[last_slot], blk_index, blk_count, reach, edge_blocks, first_block, last_block
    )
    parts = parts.at[0].add(head_in)
    parts = parts.at[last_slot].add(tail_in)
    sketch = parts.astype(jnp.bfloat16)

    product = jnp.einsum("snc,snk->ck", masked_std, sketch, preferred_element_type=jnp.float32)
    product = chunked_allreduce(product, "ind", ind_count)
    projected = product * ((1.0 - SHRINKAGE) / everyone) + SHRINKAGE * signs

    row_start = ind_index * row_slice
    my_rows = lax.dynamic_slice_in_dim(projected, row_start, row_slice, 0)
    my_slot = unit_slot[row_start // UNIT]
    pick = jnp.stack([col_slot == 0, col_slot == last_slot, col_slot == my_slot]).astype(jnp.float32)
    grams = jnp.einsum(
        "mc,ck,cl->mkl",
        pick,
        projected,
        projected,
        precision=lax.Precision.HIGHEST,
        preferred_element_type=jnp.float32,
    )
    head_in, tail_in = halo(
        grams[0], grams[1], blk_index, blk_count, reach, edge_blocks, first_block, last_block
    )
    gram = grams[2]
    gram = gram + jnp.where(my_slot == 0, head_in, 0.0)
    gram = gram + jnp.where(my_slot == last_slot, tail_in, 0.0)
    my_block = first_block + my_slot
    gram = gram / (block_units[my_block] * UNIT).astype(jnp.float32)
    return basis_rows(gram, my_rows)


def solution(mesh):
    return jax.shard_map(
        on_device,
        mesh=mesh,
        in_specs=(P("ind", "blk"), P(), P()),
        out_specs=P(("blk", "ind"), None),
        check_vma=False,
    )
```

```python
import math

import jax
import jax.numpy as jnp
from jax import lax
from jax.sharding import PartitionSpec as P

K = 256
UNIT = 128
MAX_UNITS = 32
MIN_UNITS = 4

SHRINKAGE = 0.25


def sketch_signs(columns, seed_value, lane_count):
    lane_ids = jnp.arange(lane_count, dtype=jnp.int32)
    hashed = columns[:, None] * lane_count + lane_ids[None, :]
    hashed = jnp.bitwise_xor(hashed, seed_value)
    hashed = hashed * 73244475
    hashed = jnp.bitwise_xor(hashed, jnp.right_shift(hashed, 16))
    hashed = hashed * 73244475
    hashed = jnp.bitwise_xor(hashed, jnp.right_shift(hashed, 16))
    parity = jnp.bitwise_and(jnp.right_shift(hashed, 5), 1)
    return (1 - 2 * parity).astype(jnp.float32)


def xor_allreduce(x, axis, count):
    mask = 1
    while mask < count:
        x = x + lax.ppermute(x, axis, [(j, j ^ mask) for j in range(count)])
        mask *= 2
    return x


def halving_allreduce(x, axis, count):
    place = lax.axis_index(axis)
    masks = []
    mask = 1
    while mask < count:
        masks.append(mask)
        mask *= 2
    for mask in masks:
        half = x.shape[0] // 2
        lower, upper = x[:half], x[half:]
        high = (place & mask) != 0
        send = jnp.where(high, lower, upper)
        keep = jnp.where(high, upper, lower)
        x = keep + lax.ppermute(send, axis, [(j, j ^ mask) for j in range(count)])
    for mask in reversed(masks):
        got = lax.ppermute(x, axis, [(j, j ^ mask) for j in range(count)])
        high = (place & mask) != 0
        x = jnp.where(high, jnp.concatenate([got, x], 0), jnp.concatenate([x, got], 0))
    return x


def dot_hi(a, b):
    return jnp.dot(a, b, precision=lax.Precision.HIGHEST, preferred_element_type=jnp.float32)


def lower_inverse(lower):
    eye = jnp.eye(lower.shape[0], dtype=lower.dtype)
    return jax.scipy.linalg.solve_triangular(lower, eye, lower=True)


def basis_rows(gram, rows):
    half = gram.shape[0] // 2
    l11 = jnp.linalg.cholesky(gram[:half, :half])
    m11 = lower_inverse(l11)
    l21 = dot_hi(gram[half:, :half], m11.T)
    l22 = jnp.linalg.cholesky(gram[half:, half:] - dot_hi(l21, l21.T))
    m22 = lower_inverse(l22)
    m21 = -dot_hi(m22, dot_hi(l21, m11))
    left = dot_hi(rows[:, :half], m11.T)
    right = dot_hi(rows[:, :half], m21.T) + dot_hi(rows[:, half:], m22.T)
    return jnp.concatenate([left, right], 1)


def shift(x, axis, count, step):
    pairs = [(j, j + step) for j in range(count) if 0 <= j + step < count]
    return lax.ppermute(x, axis, pairs)


def block_of(col, block_starts):
    return jnp.sum((col[..., None] >= block_starts).astype(jnp.int32), axis=-1) - 1


def halo(head_part, tail_part, blk_index, blk_count, reach, edge_blocks, first_block, last_block):
    from_lower = []
    from_upper = []
    for step in range(1, reach + 1):
        got_tail = shift(tail_part, "blk", blk_count, step)
        got_head = shift(head_part, "blk", blk_count, -step)
        lower = blk_index - step
        upper = blk_index + step
        lower_ok = jnp.logical_and(
            lower >= 0, edge_blocks[jnp.clip(lower, 0, blk_count - 1), 1] == first_block
        )
        upper_ok = jnp.logical_and(
            upper < blk_count, edge_blocks[jnp.clip(upper, 0, blk_count - 1), 0] == last_block
        )
        from_lower.append(jnp.where(lower_ok, got_tail, 0.0))
        from_upper.append(jnp.where(upper_ok, got_head, 0.0))
    return sum(from_lower[1:], from_lower[0]), sum(from_upper[1:], from_upper[0])


def on_device(genotypes, block_units, sketch_seed):
    ind_count = lax.axis_size("ind")
    blk_count = lax.axis_size("blk")
    people, col_span = genotypes.shape
    everyone = people * ind_count
    row_slice = col_span // ind_count
    unit_count = col_span // UNIT
    slot_total = (unit_count - 1) // MIN_UNITS + 2
    reach = min(-(-(MAX_UNITS - 1) // unit_count), blk_count - 1)
    blk_index = lax.axis_index("blk")
    ind_index = lax.axis_index("ind")

    dosage = genotypes.astype(jnp.float32)
    stats = xor_allreduce(jnp.stack([jnp.sum(dosage, 0), jnp.sum(dosage * dosage, 0)]), "ind", ind_count)
    average = stats[0] / everyone
    spread_sq = stats[1] / everyone - average * average
    standard = ((dosage - average) * lax.rsqrt(spread_sq + 1e-05)).astype(jnp.bfloat16)

    widths = block_units * UNIT
    block_ends = jnp.cumsum(widths, dtype=jnp.int32)
    block_starts = block_ends - widths
    col_base = blk_index * col_span
    unit_cols = col_base + jnp.arange(unit_count, dtype=jnp.int32) * UNIT
    unit_block = block_of(unit_cols, block_starts)
    first_block = unit_block[0]
    last_block = unit_block[unit_count - 1]
    unit_slot = unit_block - first_block
    group_bases = jnp.arange(blk_count, dtype=jnp.int32) * col_span
    edge_blocks = jnp.stack(
        [block_of(group_bases, block_starts), block_of(group_bases + col_span - 1, block_starts)], 1
    )
    last_slot = last_block - first_block

    columns = col_base + jnp.arange(col_span, dtype=jnp.int32)
    signs = sketch_signs(columns, sketch_seed[0], K)
    slot_ids = jnp.arange(slot_total, dtype=jnp.int32)
    col_slot = jnp.repeat(unit_slot, UNIT)
    col_mask = col_slot[None, :] == slot_ids[:, None]
    masked_std = jnp.where(col_mask[:, None, :], standard[None], jnp.zeros((), jnp.bfloat16))

    parts = jnp.einsum(
        "snc,ck->snk", masked_std, signs.astype(jnp.bfloat16), preferred_element_type=jnp.float32
    )
    head_in, tail_in = halo(
        parts[0], parts[last_slot], blk_index, blk_count, reach, edge_blocks, first_block, last_block
    )
    parts = parts.at[0].add(head_in)
    parts = parts.at[last_slot].add(tail_in)
    sketch = parts.astype(jnp.bfloat16)

    product = jnp.einsum("snc,snk->ck", masked_std, sketch, preferred_element_type=jnp.float32)
    product = halving_allreduce(product, "ind", ind_count)
    projected = product * ((1.0 - SHRINKAGE) / everyone) + SHRINKAGE * signs

    row_start = ind_index * row_slice
    my_rows = lax.dynamic_slice_in_dim(projected, row_start, row_slice, 0)
    my_slot = unit_slot[row_start // UNIT]
    pick = jnp.stack([col_slot == 0, col_slot == last_slot, col_slot == my_slot]).astype(jnp.float32)
    grams = jnp.einsum(
        "mc,ck,cl->mkl",
        pick,
        projected,
        projected,
        precision=lax.Precision.HIGHEST,
        preferred_element_type=jnp.float32,
    )
    head_in, tail_in = halo(
        grams[0], grams[1], blk_index, blk_count, reach, edge_blocks, first_block, last_block
    )
    gram = grams[2]
    gram = gram + jnp.where(my_slot == 0, head_in, 0.0)
    gram = gram + jnp.where(my_slot == last_slot, tail_in, 0.0)
    my_block = first_block + my_slot
    gram = gram / (block_units[my_block] * UNIT).astype(jnp.float32)
    return basis_rows(gram, my_rows)


def solution(mesh):
    return jax.shard_map(
        on_device,
        mesh=mesh,
        in_specs=(P("ind", "blk"), P(), P()),
        out_specs=P(("blk", "ind"), None),
        check_vma=False,
    )
```

```python
import math

import jax
import jax.numpy as jnp
from jax import lax
from jax.sharding import PartitionSpec as P

K = 256
UNIT = 128
MAX_UNITS = 32
MIN_UNITS = 4

SHRINKAGE = 0.25


def sketch_signs(columns, seed_value, lane_count):
    lane_ids = jnp.arange(lane_count, dtype=jnp.int32)
    hashed = columns[:, None] * lane_count + lane_ids[None, :]
    hashed = jnp.bitwise_xor(hashed, seed_value)
    hashed = hashed * 73244475
    hashed = jnp.bitwise_xor(hashed, jnp.right_shift(hashed, 16))
    hashed = hashed * 73244475
    hashed = jnp.bitwise_xor(hashed, jnp.right_shift(hashed, 16))
    parity = jnp.bitwise_and(jnp.right_shift(hashed, 5), 1)
    return (1 - 2 * parity).astype(jnp.float32)


def xor_allreduce(x, axis, count):
    mask = 1
    while mask < count:
        x = x + lax.ppermute(x, axis, [(j, j ^ mask) for j in range(count)])
        mask *= 2
    return x


def halving_allreduce(x, axis, count, split_masks=2):
    place = lax.axis_index(axis)
    masks = []
    mask = 1
    while mask < count:
        masks.append(mask)
        mask *= 2
    split, doubled = masks[:split_masks], masks[split_masks:]
    for mask in split:
        half = x.shape[0] // 2
        lower, upper = x[:half], x[half:]
        high = (place & mask) != 0
        send = jnp.where(high, lower, upper)
        keep = jnp.where(high, upper, lower)
        x = keep + lax.ppermute(send, axis, [(j, j ^ mask) for j in range(count)])
    for mask in doubled:
        x = x + lax.ppermute(x, axis, [(j, j ^ mask) for j in range(count)])
    for mask in reversed(split):
        got = lax.ppermute(x, axis, [(j, j ^ mask) for j in range(count)])
        high = (place & mask) != 0
        x = jnp.where(high, jnp.concatenate([got, x], 0), jnp.concatenate([x, got], 0))
    return x


def dot_hi(a, b):
    return jnp.dot(a, b, precision=lax.Precision.HIGHEST, preferred_element_type=jnp.float32)


def lower_inverse(lower):
    eye = jnp.eye(lower.shape[0], dtype=lower.dtype)
    return jax.scipy.linalg.solve_triangular(lower, eye, lower=True)


def basis_rows(gram, rows):
    half = gram.shape[0] // 2
    l11 = jnp.linalg.cholesky(gram[:half, :half])
    m11 = lower_inverse(l11)
    l21 = dot_hi(gram[half:, :half], m11.T)
    l22 = jnp.linalg.cholesky(gram[half:, half:] - dot_hi(l21, l21.T))
    m22 = lower_inverse(l22)
    m21 = -dot_hi(m22, dot_hi(l21, m11))
    left = dot_hi(rows[:, :half], m11.T)
    right = dot_hi(rows[:, :half], m21.T) + dot_hi(rows[:, half:], m22.T)
    return jnp.concatenate([left, right], 1)


def shift(x, axis, count, step):
    pairs = [(j, j + step) for j in range(count) if 0 <= j + step < count]
    return lax.ppermute(x, axis, pairs)


def block_of(col, block_starts):
    return jnp.sum((col[..., None] >= block_starts).astype(jnp.int32), axis=-1) - 1


def halo(head_part, tail_part, blk_index, blk_count, reach, edge_blocks, first_block, last_block):
    from_lower = []
    from_upper = []
    for step in range(1, reach + 1):
        got_tail = shift(tail_part, "blk", blk_count, step)
        got_head = shift(head_part, "blk", blk_count, -step)
        lower = blk_index - step
        upper = blk_index + step
        lower_ok = jnp.logical_and(
            lower >= 0, edge_blocks[jnp.clip(lower, 0, blk_count - 1), 1] == first_block
        )
        upper_ok = jnp.logical_and(
            upper < blk_count, edge_blocks[jnp.clip(upper, 0, blk_count - 1), 0] == last_block
        )
        from_lower.append(jnp.where(lower_ok, got_tail, 0.0))
        from_upper.append(jnp.where(upper_ok, got_head, 0.0))
    return sum(from_lower[1:], from_lower[0]), sum(from_upper[1:], from_upper[0])


def on_device(genotypes, block_units, sketch_seed):
    ind_count = lax.axis_size("ind")
    blk_count = lax.axis_size("blk")
    people, col_span = genotypes.shape
    everyone = people * ind_count
    row_slice = col_span // ind_count
    unit_count = col_span // UNIT
    slot_total = (unit_count - 1) // MIN_UNITS + 2
    reach = min(-(-(MAX_UNITS - 1) // unit_count), blk_count - 1)
    blk_index = lax.axis_index("blk")
    ind_index = lax.axis_index("ind")

    dosage = genotypes.astype(jnp.float32)
    stats = xor_allreduce(jnp.stack([jnp.sum(dosage, 0), jnp.sum(dosage * dosage, 0)]), "ind", ind_count)
    average = stats[0] / everyone
    spread_sq = stats[1] / everyone - average * average
    standard = ((dosage - average) * lax.rsqrt(spread_sq + 1e-05)).astype(jnp.bfloat16)

    widths = block_units * UNIT
    block_ends = jnp.cumsum(widths, dtype=jnp.int32)
    block_starts = block_ends - widths
    col_base = blk_index * col_span
    unit_cols = col_base + jnp.arange(unit_count, dtype=jnp.int32) * UNIT
    unit_block = block_of(unit_cols, block_starts)
    first_block = unit_block[0]
    last_block = unit_block[unit_count - 1]
    unit_slot = unit_block - first_block
    group_bases = jnp.arange(blk_count, dtype=jnp.int32) * col_span
    edge_blocks = jnp.stack(
        [block_of(group_bases, block_starts), block_of(group_bases + col_span - 1, block_starts)], 1
    )
    last_slot = last_block - first_block

    columns = col_base + jnp.arange(col_span, dtype=jnp.int32)
    signs = sketch_signs(columns, sketch_seed[0], K)
    slot_ids = jnp.arange(slot_total, dtype=jnp.int32)
    col_slot = jnp.repeat(unit_slot, UNIT)
    col_mask = col_slot[None, :] == slot_ids[:, None]
    masked_std = jnp.where(col_mask[:, None, :], standard[None], jnp.zeros((), jnp.bfloat16))

    parts = jnp.einsum(
        "snc,ck->snk", masked_std, signs.astype(jnp.bfloat16), preferred_element_type=jnp.float32
    )
    head_in, tail_in = halo(
        parts[0], parts[last_slot], blk_index, blk_count, reach, edge_blocks, first_block, last_block
    )
    parts = parts.at[0].add(head_in)
    parts = parts.at[last_slot].add(tail_in)
    sketch = parts.astype(jnp.bfloat16)

    product = jnp.einsum("snc,snk->ck", masked_std, sketch, preferred_element_type=jnp.float32)
    product = halving_allreduce(product, "ind", ind_count)
    projected = product * ((1.0 - SHRINKAGE) / everyone) + SHRINKAGE * signs

    row_start = ind_index * row_slice
    my_rows = lax.dynamic_slice_in_dim(projected, row_start, row_slice, 0)
    my_slot = unit_slot[row_start // UNIT]
    pick = jnp.stack([col_slot == 0, col_slot == last_slot, col_slot == my_slot]).astype(jnp.float32)
    grams = jnp.einsum(
        "mc,ck,cl->mkl",
        pick,
        projected,
        projected,
        precision=lax.Precision.HIGHEST,
        preferred_element_type=jnp.float32,
    )
    head_in, tail_in = halo(
        grams[0], grams[1], blk_index, blk_count, reach, edge_blocks, first_block, last_block
    )
    gram = grams[2]
    gram = gram + jnp.where(my_slot == 0, head_in, 0.0)
    gram = gram + jnp.where(my_slot == last_slot, tail_in, 0.0)
    my_block = first_block + my_slot
    gram = gram / (block_units[my_block] * UNIT).astype(jnp.float32)
    return basis_rows(gram, my_rows)


def solution(mesh):
    return jax.shard_map(
        on_device,
        mesh=mesh,
        in_specs=(P("ind", "blk"), P(), P()),
        out_specs=P(("blk", "ind"), None),
        check_vma=False,
    )
```

```python
import math

import jax
import jax.numpy as jnp
from jax import lax
from jax.sharding import PartitionSpec as P

K = 256
UNIT = 128
MAX_UNITS = 32
MIN_UNITS = 4

SHRINKAGE = 0.25


def sketch_signs(columns, seed_value, lane_count):
    lane_ids = jnp.arange(lane_count, dtype=jnp.int32)
    hashed = columns[:, None] * lane_count + lane_ids[None, :]
    hashed = jnp.bitwise_xor(hashed, seed_value)
    hashed = hashed * 73244475
    hashed = jnp.bitwise_xor(hashed, jnp.right_shift(hashed, 16))
    hashed = hashed * 73244475
    hashed = jnp.bitwise_xor(hashed, jnp.right_shift(hashed, 16))
    parity = jnp.bitwise_and(jnp.right_shift(hashed, 5), 1)
    return (1 - 2 * parity).astype(jnp.float32)


def xor_allreduce(x, axis, count):
    mask = 1
    while mask < count:
        x = x + lax.ppermute(x, axis, [(j, j ^ mask) for j in range(count)])
        mask *= 2
    return x


def ind_steps(count, place):
    if count % 2 or (count // 2) & (count // 2 - 1):
        steps = []
        mask = 1
        while mask < count:
            steps.append(([(j, j ^ mask) for j in range(count)], (place & mask) != 0))
            mask *= 2
        return steps
    rings = count // 2
    core = place % 2
    turned = (place // 2 + core) % rings
    steps = [([(j, j ^ 1) for j in range(count)], core != 0)]
    mask = 1
    while mask < rings:
        pairs = []
        for j in range(count):
            c, z = j % 2, j // 2
            partner = ((((z + c) % rings) ^ mask) - c) % rings
            pairs.append((j, partner * 2 + c))
        steps.append((pairs, (turned & mask) != 0))
        mask *= 2
    return steps


def halving_allreduce(x, axis, count):
    steps = ind_steps(count, lax.axis_index(axis))
    for pairs, high in steps:
        half = x.shape[0] // 2
        lower, upper = x[:half], x[half:]
        send = jnp.where(high, lower, upper)
        keep = jnp.where(high, upper, lower)
        x = keep + lax.ppermute(send, axis, pairs)
    for pairs, high in reversed(steps):
        got = lax.ppermute(x, axis, pairs)
        x = jnp.where(high, jnp.concatenate([got, x], 0), jnp.concatenate([x, got], 0))
    return x


def dot_hi(a, b):
    return jnp.dot(a, b, precision=lax.Precision.HIGHEST, preferred_element_type=jnp.float32)


def lower_inverse(lower):
    eye = jnp.eye(lower.shape[0], dtype=lower.dtype)
    return jax.scipy.linalg.solve_triangular(lower, eye, lower=True)


def basis_rows(gram, rows):
    half = gram.shape[0] // 2
    l11 = jnp.linalg.cholesky(gram[:half, :half])
    m11 = lower_inverse(l11)
    l21 = dot_hi(gram[half:, :half], m11.T)
    l22 = jnp.linalg.cholesky(gram[half:, half:] - dot_hi(l21, l21.T))
    m22 = lower_inverse(l22)
    m21 = -dot_hi(m22, dot_hi(l21, m11))
    left = dot_hi(rows[:, :half], m11.T)
    right = dot_hi(rows[:, :half], m21.T) + dot_hi(rows[:, half:], m22.T)
    return jnp.concatenate([left, right], 1)


def shift(x, axis, count, step):
    pairs = [(j, j + step) for j in range(count) if 0 <= j + step < count]
    return lax.ppermute(x, axis, pairs)


def block_of(col, block_starts):
    return jnp.sum((col[..., None] >= block_starts).astype(jnp.int32), axis=-1) - 1


def halo(head_part, tail_part, blk_index, blk_count, reach, edge_blocks, first_block, last_block):
    from_lower = []
    from_upper = []
    for step in range(1, reach + 1):
        got_tail = shift(tail_part, "blk", blk_count, step)
        got_head = shift(head_part, "blk", blk_count, -step)
        lower = blk_index - step
        upper = blk_index + step
        lower_ok = jnp.logical_and(
            lower >= 0, edge_blocks[jnp.clip(lower, 0, blk_count - 1), 1] == first_block
        )
        upper_ok = jnp.logical_and(
            upper < blk_count, edge_blocks[jnp.clip(upper, 0, blk_count - 1), 0] == last_block
        )
        from_lower.append(jnp.where(lower_ok, got_tail, 0.0))
        from_upper.append(jnp.where(upper_ok, got_head, 0.0))
    return sum(from_lower[1:], from_lower[0]), sum(from_upper[1:], from_upper[0])


def on_device(genotypes, block_units, sketch_seed):
    ind_count = lax.axis_size("ind")
    blk_count = lax.axis_size("blk")
    people, col_span = genotypes.shape
    everyone = people * ind_count
    row_slice = col_span // ind_count
    unit_count = col_span // UNIT
    slot_total = (unit_count - 1) // MIN_UNITS + 2
    reach = min(-(-(MAX_UNITS - 1) // unit_count), blk_count - 1)
    blk_index = lax.axis_index("blk")
    ind_index = lax.axis_index("ind")

    dosage = genotypes.astype(jnp.float32)
    stats = xor_allreduce(jnp.stack([jnp.sum(dosage, 0), jnp.sum(dosage * dosage, 0)]), "ind", ind_count)
    average = stats[0] / everyone
    spread_sq = stats[1] / everyone - average * average
    standard = ((dosage - average) * lax.rsqrt(spread_sq + 1e-05)).astype(jnp.bfloat16)

    widths = block_units * UNIT
    block_ends = jnp.cumsum(widths, dtype=jnp.int32)
    block_starts = block_ends - widths
    col_base = blk_index * col_span
    unit_cols = col_base + jnp.arange(unit_count, dtype=jnp.int32) * UNIT
    unit_block = block_of(unit_cols, block_starts)
    first_block = unit_block[0]
    last_block = unit_block[unit_count - 1]
    unit_slot = unit_block - first_block
    group_bases = jnp.arange(blk_count, dtype=jnp.int32) * col_span
    edge_blocks = jnp.stack(
        [block_of(group_bases, block_starts), block_of(group_bases + col_span - 1, block_starts)], 1
    )
    last_slot = last_block - first_block

    columns = col_base + jnp.arange(col_span, dtype=jnp.int32)
    signs = sketch_signs(columns, sketch_seed[0], K)
    slot_ids = jnp.arange(slot_total, dtype=jnp.int32)
    col_slot = jnp.repeat(unit_slot, UNIT)
    col_mask = col_slot[None, :] == slot_ids[:, None]
    masked_std = jnp.where(col_mask[:, None, :], standard[None], jnp.zeros((), jnp.bfloat16))

    parts = jnp.einsum(
        "snc,ck->snk", masked_std, signs.astype(jnp.bfloat16), preferred_element_type=jnp.float32
    )
    head_in, tail_in = halo(
        parts[0], parts[last_slot], blk_index, blk_count, reach, edge_blocks, first_block, last_block
    )
    parts = parts.at[0].add(head_in)
    parts = parts.at[last_slot].add(tail_in)
    sketch = parts.astype(jnp.bfloat16)

    product = jnp.einsum("snc,snk->ck", masked_std, sketch, preferred_element_type=jnp.float32)
    product = halving_allreduce(product, "ind", ind_count)
    projected = product * ((1.0 - SHRINKAGE) / everyone) + SHRINKAGE * signs

    row_start = ind_index * row_slice
    my_rows = lax.dynamic_slice_in_dim(projected, row_start, row_slice, 0)
    my_slot = unit_slot[row_start // UNIT]
    pick = jnp.stack([col_slot == 0, col_slot == last_slot, col_slot == my_slot]).astype(jnp.float32)
    grams = jnp.einsum(
        "mc,ck,cl->mkl",
        pick,
        projected,
        projected,
        precision=lax.Precision.HIGHEST,
        preferred_element_type=jnp.float32,
    )
    head_in, tail_in = halo(
        grams[0], grams[1], blk_index, blk_count, reach, edge_blocks, first_block, last_block
    )
    gram = grams[2]
    gram = gram + jnp.where(my_slot == 0, head_in, 0.0)
    gram = gram + jnp.where(my_slot == last_slot, tail_in, 0.0)
    my_block = first_block + my_slot
    gram = gram / (block_units[my_block] * UNIT).astype(jnp.float32)
    return basis_rows(gram, my_rows)


def solution(mesh):
    return jax.shard_map(
        on_device,
        mesh=mesh,
        in_specs=(P("ind", "blk"), P(), P()),
        out_specs=P(("blk", "ind"), None),
        check_vma=False,
    )
```

```python
import math

import jax
import jax.numpy as jnp
from jax import lax
from jax.sharding import PartitionSpec as P

K = 256
UNIT = 128
MAX_UNITS = 32
MIN_UNITS = 4

SHRINKAGE = 0.25


def sketch_signs(columns, seed_value, lane_count):
    lane_ids = jnp.arange(lane_count, dtype=jnp.int32)
    hashed = columns[:, None] * lane_count + lane_ids[None, :]
    hashed = jnp.bitwise_xor(hashed, seed_value)
    hashed = hashed * 73244475
    hashed = jnp.bitwise_xor(hashed, jnp.right_shift(hashed, 16))
    hashed = hashed * 73244475
    hashed = jnp.bitwise_xor(hashed, jnp.right_shift(hashed, 16))
    parity = jnp.bitwise_and(jnp.right_shift(hashed, 5), 1)
    return (1 - 2 * parity).astype(jnp.float32)


def xor_allreduce(x, axis, count):
    mask = 1
    while mask < count:
        x = x + lax.ppermute(x, axis, [(j, j ^ mask) for j in range(count)])
        mask *= 2
    return x


def ind_steps(count, place):
    if count % 2 or (count // 2) & (count // 2 - 1):
        steps = []
        mask = 1
        while mask < count:
            steps.append(([(j, j ^ mask) for j in range(count)], (place & mask) != 0))
            mask *= 2
        return steps
    rings = count // 2
    core = place % 2
    turned = (place // 2 + core) % rings
    steps = [([(j, j ^ 1) for j in range(count)], core != 0)]
    mask = 1
    while mask < rings:
        pairs = []
        for j in range(count):
            c, z = j % 2, j // 2
            partner = ((((z + c) % rings) ^ mask) - c) % rings
            pairs.append((j, partner * 2 + c))
        steps.append((pairs, (turned & mask) != 0))
        mask *= 2
    return steps


def halving_allreduce(x, axis, count):
    steps = ind_steps(count, lax.axis_index(axis))
    for pairs, high in steps:
        half = x.shape[0] // 2
        lower, upper = x[:half], x[half:]
        send = jnp.where(high, lower, upper)
        keep = jnp.where(high, upper, lower)
        x = keep + lax.ppermute(send, axis, pairs)
    for pairs, high in reversed(steps):
        got = lax.ppermute(x, axis, pairs)
        x = jnp.where(high, jnp.concatenate([got, x], 0), jnp.concatenate([x, got], 0))
    return x


def dot_hi(a, b):
    return jnp.dot(a, b, precision=lax.Precision.HIGHEST, preferred_element_type=jnp.float32)


def lower_inverse(lower):
    eye = jnp.eye(lower.shape[0], dtype=lower.dtype)
    return jax.scipy.linalg.solve_triangular(lower, eye, lower=True)


def basis_rows(gram, rows):
    half = gram.shape[0] // 2
    l11 = jnp.linalg.cholesky(gram[:half, :half])
    m11 = lower_inverse(l11)
    l21 = dot_hi(gram[half:, :half], m11.T)
    l22 = jnp.linalg.cholesky(gram[half:, half:] - dot_hi(l21, l21.T))
    m22 = lower_inverse(l22)
    m21 = -dot_hi(m22, dot_hi(l21, m11))
    left = dot_hi(rows[:, :half], m11.T)
    right = dot_hi(rows[:, :half], m21.T) + dot_hi(rows[:, half:], m22.T)
    return jnp.concatenate([left, right], 1)


def shift(x, axis, count, step):
    pairs = [(j, j + step) for j in range(count) if 0 <= j + step < count]
    return lax.ppermute(x, axis, pairs)


def block_of(col, block_starts):
    return jnp.sum((col[..., None] >= block_starts).astype(jnp.int32), axis=-1) - 1


def halo(head_part, tail_part, blk_index, blk_count, reach, edge_blocks, first_block, last_block):
    head_part, tail_part = lax.optimization_barrier((head_part, tail_part))
    from_lower = []
    from_upper = []
    for step in range(1, reach + 1):
        got_tail = shift(tail_part, "blk", blk_count, step)
        got_head = shift(head_part, "blk", blk_count, -step)
        lower = blk_index - step
        upper = blk_index + step
        lower_ok = jnp.logical_and(
            lower >= 0, edge_blocks[jnp.clip(lower, 0, blk_count - 1), 1] == first_block
        )
        upper_ok = jnp.logical_and(
            upper < blk_count, edge_blocks[jnp.clip(upper, 0, blk_count - 1), 0] == last_block
        )
        from_lower.append(jnp.where(lower_ok, got_tail, 0.0))
        from_upper.append(jnp.where(upper_ok, got_head, 0.0))
    return sum(from_lower[1:], from_lower[0]), sum(from_upper[1:], from_upper[0])


def on_device(genotypes, block_units, sketch_seed):
    ind_count = lax.axis_size("ind")
    blk_count = lax.axis_size("blk")
    people, col_span = genotypes.shape
    everyone = people * ind_count
    row_slice = col_span // ind_count
    unit_count = col_span // UNIT
    slot_total = (unit_count - 1) // MIN_UNITS + 2
    reach = min(-(-(MAX_UNITS - 1) // unit_count), blk_count - 1)
    blk_index = lax.axis_index("blk")
    ind_index = lax.axis_index("ind")

    dosage = genotypes.astype(jnp.float32)
    stats = xor_allreduce(jnp.stack([jnp.sum(dosage, 0), jnp.sum(dosage * dosage, 0)]), "ind", ind_count)
    average = stats[0] / everyone
    spread_sq = stats[1] / everyone - average * average
    standard = ((dosage - average) * lax.rsqrt(spread_sq + 1e-05)).astype(jnp.bfloat16)

    widths = block_units * UNIT
    block_ends = jnp.cumsum(widths, dtype=jnp.int32)
    block_starts = block_ends - widths
    col_base = blk_index * col_span
    unit_cols = col_base + jnp.arange(unit_count, dtype=jnp.int32) * UNIT
    unit_block = block_of(unit_cols, block_starts)
    first_block = unit_block[0]
    last_block = unit_block[unit_count - 1]
    unit_slot = unit_block - first_block
    group_bases = jnp.arange(blk_count, dtype=jnp.int32) * col_span
    edge_blocks = jnp.stack(
        [block_of(group_bases, block_starts), block_of(group_bases + col_span - 1, block_starts)], 1
    )
    last_slot = last_block - first_block

    columns = col_base + jnp.arange(col_span, dtype=jnp.int32)
    signs = sketch_signs(columns, sketch_seed[0], K)
    slot_ids = jnp.arange(slot_total, dtype=jnp.int32)
    col_slot = jnp.repeat(unit_slot, UNIT)
    col_mask = col_slot[None, :] == slot_ids[:, None]
    masked_std = jnp.where(col_mask[:, None, :], standard[None], jnp.zeros((), jnp.bfloat16))

    parts = jnp.einsum(
        "snc,ck->snk", masked_std, signs.astype(jnp.bfloat16), preferred_element_type=jnp.float32
    )
    head_in, tail_in = halo(
        parts[0], parts[last_slot], blk_index, blk_count, reach, edge_blocks, first_block, last_block
    )
    parts = parts.at[0].add(head_in)
    parts = parts.at[last_slot].add(tail_in)
    sketch = parts.astype(jnp.bfloat16)

    product = jnp.einsum("snc,snk->ck", masked_std, sketch, preferred_element_type=jnp.float32)
    product = halving_allreduce(product, "ind", ind_count)
    projected = product * ((1.0 - SHRINKAGE) / everyone) + SHRINKAGE * signs

    row_start = ind_index * row_slice
    my_rows = lax.dynamic_slice_in_dim(projected, row_start, row_slice, 0)
    my_slot = unit_slot[row_start // UNIT]
    unit_grams = jnp.einsum(
        "tgk,tgl->tkl",
        projected.reshape(unit_count, UNIT, K),
        projected.reshape(unit_count, UNIT, K),
        precision=lax.Precision.HIGHEST,
        preferred_element_type=jnp.float32,
    )
    pick = jnp.stack([unit_slot == 0, unit_slot == last_slot, unit_slot == my_slot]).astype(jnp.float32)
    grams = jnp.einsum(
        "mt,tkl->mkl",
        pick,
        unit_grams,
        precision=lax.Precision.HIGHEST,
        preferred_element_type=jnp.float32,
    )
    head_in, tail_in = halo(
        grams[0], grams[1], blk_index, blk_count, reach, edge_blocks, first_block, last_block
    )
    gram = grams[2]
    gram = gram + jnp.where(my_slot == 0, head_in, 0.0)
    gram = gram + jnp.where(my_slot == last_slot, tail_in, 0.0)
    my_block = first_block + my_slot
    gram = gram / (block_units[my_block] * UNIT).astype(jnp.float32)
    return basis_rows(gram, my_rows)


def solution(mesh):
    return jax.shard_map(
        on_device,
        mesh=mesh,
        in_specs=(P("ind", "blk"), P(), P()),
        out_specs=P(("blk", "ind"), None),
        check_vma=False,
    )
```

```python
import math

import jax
import jax.numpy as jnp
from jax import lax
from jax.sharding import PartitionSpec as P

K = 256
UNIT = 128
MAX_UNITS = 32
MIN_UNITS = 4

SHRINKAGE = 0.25


def sketch_signs(columns, seed_value, lane_count):
    lane_ids = jnp.arange(lane_count, dtype=jnp.int32)
    hashed = columns[:, None] * lane_count + lane_ids[None, :]
    hashed = jnp.bitwise_xor(hashed, seed_value)
    hashed = hashed * 73244475
    hashed = jnp.bitwise_xor(hashed, jnp.right_shift(hashed, 16))
    hashed = hashed * 73244475
    hashed = jnp.bitwise_xor(hashed, jnp.right_shift(hashed, 16))
    parity = jnp.bitwise_and(jnp.right_shift(hashed, 5), 1)
    return (1 - 2 * parity).astype(jnp.float32)


def xor_allreduce(x, axis, count):
    mask = 1
    while mask < count:
        x = x + lax.ppermute(x, axis, [(j, j ^ mask) for j in range(count)])
        mask *= 2
    return x


def ind_steps(count, place):
    if count % 2 or (count // 2) & (count // 2 - 1):
        steps = []
        mask = 1
        while mask < count:
            steps.append(([(j, j ^ mask) for j in range(count)], (place & mask) != 0))
            mask *= 2
        return steps
    rings = count // 2
    core = place % 2
    turned = (place // 2 + core) % rings
    steps = [([(j, j ^ 1) for j in range(count)], core != 0)]
    mask = 1
    while mask < rings:
        pairs = []
        for j in range(count):
            c, z = j % 2, j // 2
            partner = ((((z + c) % rings) ^ mask) - c) % rings
            pairs.append((j, partner * 2 + c))
        steps.append((pairs, (turned & mask) != 0))
        mask *= 2
    return steps


def halving_allreduce(x, axis, count, doubled_steps=1):
    steps = ind_steps(count, lax.axis_index(axis))
    split, doubled = steps[: len(steps) - doubled_steps], steps[len(steps) - doubled_steps :]
    for pairs, high in split:
        half = x.shape[0] // 2
        lower, upper = x[:half], x[half:]
        send = jnp.where(high, lower, upper)
        keep = jnp.where(high, upper, lower)
        x = keep + lax.ppermute(send, axis, pairs)
    for pairs, high in doubled:
        x = x + lax.ppermute(x, axis, pairs)
    for pairs, high in reversed(split):
        got = lax.ppermute(x, axis, pairs)
        x = jnp.where(high, jnp.concatenate([got, x], 0), jnp.concatenate([x, got], 0))
    return x


def dot_hi(a, b):
    return jnp.dot(a, b, precision=lax.Precision.HIGHEST, preferred_element_type=jnp.float32)


def lower_inverse(lower):
    eye = jnp.eye(lower.shape[0], dtype=lower.dtype)
    return jax.scipy.linalg.solve_triangular(lower, eye, lower=True)


def basis_rows(gram, rows):
    half = gram.shape[0] // 2
    l11 = jnp.linalg.cholesky(gram[:half, :half])
    m11 = lower_inverse(l11)
    l21 = dot_hi(gram[half:, :half], m11.T)
    l22 = jnp.linalg.cholesky(gram[half:, half:] - dot_hi(l21, l21.T))
    m22 = lower_inverse(l22)
    m21 = -dot_hi(m22, dot_hi(l21, m11))
    left = dot_hi(rows[:, :half], m11.T)
    right = dot_hi(rows[:, :half], m21.T) + dot_hi(rows[:, half:], m22.T)
    return jnp.concatenate([left, right], 1)


def shift(x, axis, count, step):
    pairs = [(j, j + step) for j in range(count) if 0 <= j + step < count]
    return lax.ppermute(x, axis, pairs)


def block_of(col, block_starts):
    return jnp.sum((col[..., None] >= block_starts).astype(jnp.int32), axis=-1) - 1


def halo(head_part, tail_part, blk_index, blk_count, reach, edge_blocks, first_block, last_block):
    head_part, tail_part = lax.optimization_barrier((head_part, tail_part))
    from_lower = []
    from_upper = []
    for step in range(1, reach + 1):
        got_tail = shift(tail_part, "blk", blk_count, step)
        got_head = shift(head_part, "blk", blk_count, -step)
        lower = blk_index - step
        upper = blk_index + step
        lower_ok = jnp.logical_and(
            lower >= 0, edge_blocks[jnp.clip(lower, 0, blk_count - 1), 1] == first_block
        )
        upper_ok = jnp.logical_and(
            upper < blk_count, edge_blocks[jnp.clip(upper, 0, blk_count - 1), 0] == last_block
        )
        from_lower.append(jnp.where(lower_ok, got_tail, 0.0))
        from_upper.append(jnp.where(upper_ok, got_head, 0.0))
    return sum(from_lower[1:], from_lower[0]), sum(from_upper[1:], from_upper[0])


def on_device(genotypes, block_units, sketch_seed):
    ind_count = lax.axis_size("ind")
    blk_count = lax.axis_size("blk")
    people, col_span = genotypes.shape
    everyone = people * ind_count
    row_slice = col_span // ind_count
    unit_count = col_span // UNIT
    slot_total = (unit_count - 1) // MIN_UNITS + 2
    reach = min(-(-(MAX_UNITS - 1) // unit_count), blk_count - 1)
    blk_index = lax.axis_index("blk")
    ind_index = lax.axis_index("ind")

    dosage = genotypes.astype(jnp.float32)
    stats = xor_allreduce(jnp.stack([jnp.sum(dosage, 0), jnp.sum(dosage * dosage, 0)]), "ind", ind_count)
    average = stats[0] / everyone
    spread_sq = stats[1] / everyone - average * average
    standard = ((dosage - average) * lax.rsqrt(spread_sq + 1e-05)).astype(jnp.bfloat16)

    widths = block_units * UNIT
    block_ends = jnp.cumsum(widths, dtype=jnp.int32)
    block_starts = block_ends - widths
    col_base = blk_index * col_span
    unit_cols = col_base + jnp.arange(unit_count, dtype=jnp.int32) * UNIT
    unit_block = block_of(unit_cols, block_starts)
    first_block = unit_block[0]
    last_block = unit_block[unit_count - 1]
    unit_slot = unit_block - first_block
    group_bases = jnp.arange(blk_count, dtype=jnp.int32) * col_span
    edge_blocks = jnp.stack(
        [block_of(group_bases, block_starts), block_of(group_bases + col_span - 1, block_starts)], 1
    )
    last_slot = last_block - first_block

    columns = col_base + jnp.arange(col_span, dtype=jnp.int32)
    signs = sketch_signs(columns, sketch_seed[0], K)
    slot_ids = jnp.arange(slot_total, dtype=jnp.int32)
    col_slot = jnp.repeat(unit_slot, UNIT)
    col_mask = col_slot[None, :] == slot_ids[:, None]
    masked_std = jnp.where(col_mask[:, None, :], standard[None], jnp.zeros((), jnp.bfloat16))

    parts = jnp.einsum(
        "snc,ck->snk", masked_std, signs.astype(jnp.bfloat16), preferred_element_type=jnp.float32
    )
    head_in, tail_in = halo(
        parts[0], parts[last_slot], blk_index, blk_count, reach, edge_blocks, first_block, last_block
    )
    parts = parts.at[0].add(head_in)
    parts = parts.at[last_slot].add(tail_in)
    sketch = parts.astype(jnp.bfloat16)

    product = jnp.einsum("snc,snk->ck", masked_std, sketch, preferred_element_type=jnp.float32)
    product = halving_allreduce(product, "ind", ind_count)
    projected = product * ((1.0 - SHRINKAGE) / everyone) + SHRINKAGE * signs

    row_start = ind_index * row_slice
    my_rows = lax.dynamic_slice_in_dim(projected, row_start, row_slice, 0)
    my_slot = unit_slot[row_start // UNIT]
    edges = jnp.stack([col_slot == 0, col_slot == last_slot]).astype(jnp.float32)
    grams = jnp.einsum(
        "mc,ck,cl->mkl",
        edges,
        projected,
        projected,
        precision=lax.Precision.HIGHEST,
        preferred_element_type=jnp.float32,
    )
    head_in, tail_in = halo(
        grams[0], grams[1], blk_index, blk_count, reach, edge_blocks, first_block, last_block
    )
    own = (col_slot == my_slot).astype(jnp.float32)
    gram = jnp.einsum(
        "c,ck,cl->kl",
        own,
        projected,
        projected,
        precision=lax.Precision.HIGHEST,
        preferred_element_type=jnp.float32,
    )
    gram = gram + jnp.where(my_slot == 0, head_in, 0.0)
    gram = gram + jnp.where(my_slot == last_slot, tail_in, 0.0)
    my_block = first_block + my_slot
    gram = gram / (block_units[my_block] * UNIT).astype(jnp.float32)
    return basis_rows(gram, my_rows)


def solution(mesh):
    return jax.shard_map(
        on_device,
        mesh=mesh,
        in_specs=(P("ind", "blk"), P(), P()),
        out_specs=P(("blk", "ind"), None),
        check_vma=False,
    )
```

```python
import jax
import jax.numpy as jnp
from jax import lax
from jax.sharding import PartitionSpec as P


K = 256
UNIT = 128
MAX_UNITS = 32
MIN_UNITS = 4

SHRINKAGE = 0.25


def sketch_signs(columns, seed_value, lane_count):
    lane_ids = jnp.arange(lane_count, dtype=jnp.int32)
    hashed = columns[:, None] * lane_count + lane_ids[None, :]
    hashed = jnp.bitwise_xor(hashed, seed_value)
    hashed = hashed * 73244475
    hashed = jnp.bitwise_xor(hashed, jnp.right_shift(hashed, 16))
    hashed = hashed * 73244475
    hashed = jnp.bitwise_xor(hashed, jnp.right_shift(hashed, 16))
    parity = jnp.bitwise_and(jnp.right_shift(hashed, 5), 1)
    return (1 - 2 * parity).astype(jnp.float32)


def xor_allreduce(x, axis, count):
    mask = 1
    while mask < count:
        x = x + lax.ppermute(x, axis, [(j, j ^ mask) for j in range(count)])
        mask *= 2
    return x


def ind_steps(count, place):
    if count % 2 or (count // 2) & (count // 2 - 1):
        steps = []
        mask = 1
        while mask < count:
            steps.append(([(j, j ^ mask) for j in range(count)], (place & mask) != 0))
            mask *= 2
        return steps
    rings = count // 2
    core = place % 2
    turned = (place // 2 + core) % rings
    steps = [([(j, j ^ 1) for j in range(count)], core != 0)]
    mask = 1
    while mask < rings:
        pairs = []
        for j in range(count):
            c, z = j % 2, j // 2
            partner = ((((z + c) % rings) ^ mask) - c) % rings
            pairs.append((j, partner * 2 + c))
        steps.append((pairs, (turned & mask) != 0))
        mask *= 2
    return steps


def halving_allreduce(x, axis, count, doubled_steps=1):
    steps = ind_steps(count, lax.axis_index(axis))
    split, doubled = steps[: len(steps) - doubled_steps], steps[len(steps) - doubled_steps :]
    for pairs, high in split:
        half = x.shape[0] // 2
        lower, upper = x[:half], x[half:]
        send = jnp.where(high, lower, upper)
        keep = jnp.where(high, upper, lower)
        x = keep + lax.ppermute(send, axis, pairs)
    for pairs, high in doubled:
        x = x + lax.ppermute(x, axis, pairs)
    for pairs, high in reversed(split):
        got = lax.ppermute(x, axis, pairs)
        x = jnp.where(high, jnp.concatenate([got, x], 0), jnp.concatenate([x, got], 0))
    return x


def dot_hi(a, b):
    return jnp.dot(a, b, precision=lax.Precision.HIGHEST, preferred_element_type=jnp.float32)


def lower_inverse(lower):
    eye = jnp.eye(lower.shape[0], dtype=lower.dtype)
    return jax.scipy.linalg.solve_triangular(lower, eye, lower=True)


def basis_rows(gram, rows):
    half = gram.shape[0] // 2
    l11 = lax.linalg.cholesky(gram[:half, :half], symmetrize_input=False)
    m11 = lower_inverse(l11)
    l21 = dot_hi(gram[half:, :half], m11.T)
    l22 = lax.linalg.cholesky(gram[half:, half:] - dot_hi(l21, l21.T), symmetrize_input=False)
    m22 = lower_inverse(l22)
    m21 = -dot_hi(m22, dot_hi(l21, m11))
    left = dot_hi(rows[:, :half], m11.T)
    right = dot_hi(rows[:, :half], m21.T) + dot_hi(rows[:, half:], m22.T)
    return jnp.concatenate([left, right], 1)


def pack_symmetric(gram):
    half = gram.shape[0] // 2
    corner = gram[half:, half:].reshape(half // 2, gram.shape[1])
    return jnp.concatenate([gram[:half], corner], 0)


def unpack_symmetric(packed):
    half = packed.shape[1] // 2
    top = packed[:half]
    corner = packed[half:].reshape(half, half)
    bottom = jnp.concatenate([top[:, half:].T, corner], 1)
    return jnp.concatenate([top, bottom], 0)


def shift(x, axis, count, step):
    pairs = [(j, j + step) for j in range(count) if 0 <= j + step < count]
    return lax.ppermute(x, axis, pairs)


def block_of(col, block_starts):
    return jnp.sum((col[..., None] >= block_starts).astype(jnp.int32), axis=-1) - 1


def halo(head_part, tail_part, blk_index, blk_count, reach, edge_blocks, first_block, last_block):
    head_part, tail_part = lax.optimization_barrier((head_part, tail_part))
    from_lower = []
    from_upper = []
    for step in range(1, reach + 1):
        got_tail = shift(tail_part, "blk", blk_count, step)
        got_head = shift(head_part, "blk", blk_count, -step)
        lower = blk_index - step
        upper = blk_index + step
        lower_ok = jnp.logical_and(
            lower >= 0, edge_blocks[jnp.clip(lower, 0, blk_count - 1), 1] == first_block
        )
        upper_ok = jnp.logical_and(
            upper < blk_count, edge_blocks[jnp.clip(upper, 0, blk_count - 1), 0] == last_block
        )
        from_lower.append(jnp.where(lower_ok, got_tail, 0.0))
        from_upper.append(jnp.where(upper_ok, got_head, 0.0))
    return sum(from_lower[1:], from_lower[0]), sum(from_upper[1:], from_upper[0])


def on_device(genotypes, block_units, sketch_seed):
    ind_count = lax.axis_size("ind")
    blk_count = lax.axis_size("blk")
    people, col_span = genotypes.shape
    everyone = people * ind_count
    row_slice = col_span // ind_count
    unit_count = col_span // UNIT
    slot_total = (unit_count - 1) // MIN_UNITS + 2
    reach = min(-(-(MAX_UNITS - 1) // unit_count), blk_count - 1)
    blk_index = lax.axis_index("blk")
    ind_index = lax.axis_index("ind")

    dosage = genotypes.astype(jnp.float32)
    stats = xor_allreduce(jnp.stack([jnp.sum(dosage, 0), jnp.sum(dosage * dosage, 0)]), "ind", ind_count)
    average = stats[0] / everyone
    spread_sq = stats[1] / everyone - average * average
    standard = ((dosage - average) * lax.rsqrt(spread_sq + 1e-05)).astype(jnp.bfloat16)

    widths = block_units * UNIT
    block_ends = jnp.cumsum(widths, dtype=jnp.int32)
    block_starts = block_ends - widths
    col_base = blk_index * col_span
    unit_cols = col_base + jnp.arange(unit_count, dtype=jnp.int32) * UNIT
    unit_block = block_of(unit_cols, block_starts)
    first_block = unit_block[0]
    last_block = unit_block[unit_count - 1]
    unit_slot = unit_block - first_block
    group_bases = jnp.arange(blk_count, dtype=jnp.int32) * col_span
    edge_blocks = jnp.stack(
        [block_of(group_bases, block_starts), block_of(group_bases + col_span - 1, block_starts)], 1
    )
    last_slot = last_block - first_block

    columns = col_base + jnp.arange(col_span, dtype=jnp.int32)
    signs = sketch_signs(columns, sketch_seed[0], K)
    slot_ids = jnp.arange(slot_total, dtype=jnp.int32)
    col_slot = jnp.repeat(unit_slot, UNIT)
    col_mask = col_slot[None, :] == slot_ids[:, None]
    masked_std = jnp.where(col_mask[:, None, :], standard[None], jnp.zeros((), jnp.bfloat16))

    parts = jnp.einsum(
        "snc,ck->snk", masked_std, signs.astype(jnp.bfloat16), preferred_element_type=jnp.float32
    )
    head_in, tail_in = halo(
        parts[0], parts[last_slot], blk_index, blk_count, reach, edge_blocks, first_block, last_block
    )
    parts = parts.at[0].add(head_in)
    parts = parts.at[last_slot].add(tail_in)
    sketch = parts.astype(jnp.bfloat16)

    product = jnp.einsum("snc,snk->ck", masked_std, sketch, preferred_element_type=jnp.float32)
    product = halving_allreduce(product, "ind", ind_count)
    projected = product * ((1.0 - SHRINKAGE) / everyone) + SHRINKAGE * signs

    row_start = ind_index * row_slice
    my_rows = lax.dynamic_slice_in_dim(projected, row_start, row_slice, 0)
    my_slot = unit_slot[row_start // UNIT]
    edges = jnp.stack([col_slot == 0, col_slot == last_slot]).astype(jnp.float32)
    grams = jnp.einsum(
        "mc,ck,cl->mkl",
        edges,
        projected,
        projected,
        precision=lax.Precision.HIGHEST,
        preferred_element_type=jnp.float32,
    )
    head_in, tail_in = halo(
        pack_symmetric(grams[0]),
        pack_symmetric(grams[1]),
        blk_index,
        blk_count,
        reach,
        edge_blocks,
        first_block,
        last_block,
    )
    head_in = unpack_symmetric(head_in)
    tail_in = unpack_symmetric(tail_in)
    own = (col_slot == my_slot).astype(jnp.float32)
    gram = jnp.einsum(
        "c,ck,cl->kl",
        own,
        projected,
        projected,
        precision=lax.Precision.HIGHEST,
        preferred_element_type=jnp.float32,
    )
    gram = lax.optimization_barrier(gram)
    gram = gram + jnp.where(my_slot == 0, head_in, 0.0)
    gram = gram + jnp.where(my_slot == last_slot, tail_in, 0.0)
    my_block = first_block + my_slot
    gram = gram / (block_units[my_block] * UNIT).astype(jnp.float32)
    return basis_rows(gram, my_rows)


def solution(mesh):
    return jax.shard_map(
        on_device,
        mesh=mesh,
        in_specs=(P("ind", "blk"), P(), P()),
        out_specs=P(("blk", "ind"), None),
        check_vma=False,
    )
```

```python
import jax
import jax.numpy as jnp
from jax import lax
from jax.sharding import PartitionSpec as P


K = 256
UNIT = 128
MAX_UNITS = 32
MIN_UNITS = 4

SHRINKAGE = 0.25


def sketch_signs(columns, seed_value, lane_count):
    lane_ids = jnp.arange(lane_count, dtype=jnp.int32)
    hashed = columns[:, None] * lane_count + lane_ids[None, :]
    hashed = jnp.bitwise_xor(hashed, seed_value)
    hashed = hashed * 73244475
    hashed = jnp.bitwise_xor(hashed, jnp.right_shift(hashed, 16))
    hashed = hashed * 73244475
    hashed = jnp.bitwise_xor(hashed, jnp.right_shift(hashed, 16))
    parity = jnp.bitwise_and(jnp.right_shift(hashed, 5), 1)
    return (1 - 2 * parity).astype(jnp.float32)


def xor_allreduce(x, axis, count):
    mask = 1
    while mask < count:
        x = x + lax.ppermute(x, axis, [(j, j ^ mask) for j in range(count)])
        mask *= 2
    return x


def ind_steps(count, place):
    if count % 2 or (count // 2) & (count // 2 - 1):
        steps = []
        mask = 1
        while mask < count:
            steps.append(([(j, j ^ mask) for j in range(count)], (place & mask) != 0))
            mask *= 2
        return steps
    rings = count // 2
    core = place % 2
    turned = (place // 2 + core) % rings
    steps = [([(j, j ^ 1) for j in range(count)], core != 0)]
    mask = 1
    while mask < rings:
        pairs = []
        for j in range(count):
            c, z = j % 2, j // 2
            partner = ((((z + c) % rings) ^ mask) - c) % rings
            pairs.append((j, partner * 2 + c))
        steps.append((pairs, (turned & mask) != 0))
        mask *= 2
    return steps


def halving_allreduce(x, axis, count, doubled_steps=1):
    steps = ind_steps(count, lax.axis_index(axis))
    split, doubled = steps[: len(steps) - doubled_steps], steps[len(steps) - doubled_steps :]
    for pairs, high in split:
        half = x.shape[0] // 2
        lower, upper = x[:half], x[half:]
        send = jnp.where(high, lower, upper)
        keep = jnp.where(high, upper, lower)
        x = keep + lax.ppermute(send, axis, pairs)
    for pairs, high in doubled:
        x = x + lax.ppermute(x, axis, pairs)
    for pairs, high in reversed(split):
        got = lax.ppermute(x, axis, pairs)
        x = jnp.where(high, jnp.concatenate([got, x], 0), jnp.concatenate([x, got], 0))
    return x


def dot_hi(a, b):
    return jnp.dot(a, b, precision=lax.Precision.HIGHEST, preferred_element_type=jnp.float32)


def lower_inverse(lower):
    eye = jnp.eye(lower.shape[0], dtype=lower.dtype)
    return jax.scipy.linalg.solve_triangular(lower, eye, lower=True)


def basis_rows(gram, rows):
    half = gram.shape[0] // 2
    l11 = jnp.linalg.cholesky(gram[:half, :half])
    m11 = lower_inverse(l11)
    l21 = dot_hi(gram[half:, :half], m11.T)
    l22 = jnp.linalg.cholesky(gram[half:, half:] - dot_hi(l21, l21.T))
    m22 = lower_inverse(l22)
    m21 = -dot_hi(m22, dot_hi(l21, m11))
    left = dot_hi(rows[:, :half], m11.T)
    right = dot_hi(rows[:, :half], m21.T) + dot_hi(rows[:, half:], m22.T)
    return jnp.concatenate([left, right], 1)


def pack_symmetric(gram):
    half = gram.shape[0] // 2
    corner = gram[half:, half:].reshape(half // 2, gram.shape[1])
    return jnp.concatenate([gram[:half], corner], 0)


def unpack_symmetric(packed):
    half = packed.shape[1] // 2
    top = packed[:half]
    corner = packed[half:].reshape(half, half)
    bottom = jnp.concatenate([top[:, half:].T, corner], 1)
    return jnp.concatenate([top, bottom], 0)


def shift(x, axis, count, step):
    pairs = [(j, j + step) for j in range(count) if 0 <= j + step < count]
    return lax.ppermute(x, axis, pairs)


def block_of(col, block_starts):
    return jnp.sum((col[..., None] >= block_starts).astype(jnp.int32), axis=-1) - 1


def halo(head_part, tail_part, blk_index, blk_count, reach, edge_blocks, first_block, last_block):
    head_part, tail_part = lax.optimization_barrier((head_part, tail_part))
    from_lower = []
    from_upper = []
    for step in range(1, reach + 1):
        got_tail = shift(tail_part, "blk", blk_count, step)
        got_head = shift(head_part, "blk", blk_count, -step)
        lower = blk_index - step
        upper = blk_index + step
        lower_ok = jnp.logical_and(
            lower >= 0, edge_blocks[jnp.clip(lower, 0, blk_count - 1), 1] == first_block
        )
        upper_ok = jnp.logical_and(
            upper < blk_count, edge_blocks[jnp.clip(upper, 0, blk_count - 1), 0] == last_block
        )
        from_lower.append(jnp.where(lower_ok, got_tail, 0.0))
        from_upper.append(jnp.where(upper_ok, got_head, 0.0))
    return sum(from_lower[1:], from_lower[0]), sum(from_upper[1:], from_upper[0])


def on_device(genotypes, block_units, sketch_seed):
    ind_count = lax.axis_size("ind")
    blk_count = lax.axis_size("blk")
    people, col_span = genotypes.shape
    everyone = people * ind_count
    row_slice = col_span // ind_count
    unit_count = col_span // UNIT
    slot_total = (unit_count - 1) // MIN_UNITS + 2
    reach = min(-(-(MAX_UNITS - 1) // unit_count), blk_count - 1)
    blk_index = lax.axis_index("blk")
    ind_index = lax.axis_index("ind")

    dosage = genotypes.astype(jnp.float32)
    stats = xor_allreduce(jnp.stack([jnp.sum(dosage, 0), jnp.sum(dosage * dosage, 0)]), "ind", ind_count)
    average = stats[0] / everyone
    spread_sq = stats[1] / everyone - average * average
    standard = ((dosage - average) * lax.rsqrt(spread_sq + 1e-05)).astype(jnp.bfloat16)

    widths = block_units * UNIT
    block_ends = jnp.cumsum(widths, dtype=jnp.int32)
    block_starts = block_ends - widths
    col_base = blk_index * col_span
    unit_cols = col_base + jnp.arange(unit_count, dtype=jnp.int32) * UNIT
    unit_block = block_of(unit_cols, block_starts)
    first_block = unit_block[0]
    last_block = unit_block[unit_count - 1]
    unit_slot = unit_block - first_block
    group_bases = jnp.arange(blk_count, dtype=jnp.int32) * col_span
    edge_blocks = jnp.stack(
        [block_of(group_bases, block_starts), block_of(group_bases + col_span - 1, block_starts)], 1
    )
    last_slot = last_block - first_block

    columns = col_base + jnp.arange(col_span, dtype=jnp.int32)
    signs = sketch_signs(columns, sketch_seed[0], K)
    signs_b = signs.astype(jnp.bfloat16)
    signs, signs_b = lax.optimization_barrier((signs, signs_b))
    slot_ids = jnp.arange(slot_total, dtype=jnp.int32)
    col_slot = jnp.repeat(unit_slot, UNIT)
    col_mask = col_slot[None, :] == slot_ids[:, None]
    masked_std = jnp.where(col_mask[:, None, :], standard[None], jnp.zeros((), jnp.bfloat16))

    parts = jnp.einsum(
        "snc,ck->snk", masked_std, signs_b, preferred_element_type=jnp.float32
    )
    head_in, tail_in = halo(
        parts[0], parts[last_slot], blk_index, blk_count, reach, edge_blocks, first_block, last_block
    )
    parts = parts.at[0].add(head_in)
    parts = parts.at[last_slot].add(tail_in)
    sketch = parts.astype(jnp.bfloat16)

    product = jnp.einsum("snc,snk->ck", masked_std, sketch, preferred_element_type=jnp.float32)
    product = halving_allreduce(product, "ind", ind_count)
    projected = product * ((1.0 - SHRINKAGE) / everyone) + SHRINKAGE * signs

    row_start = ind_index * row_slice
    my_rows = lax.dynamic_slice_in_dim(projected, row_start, row_slice, 0)
    my_slot = unit_slot[row_start // UNIT]
    edges = jnp.stack([col_slot == 0, col_slot == last_slot]).astype(jnp.float32)
    grams = jnp.einsum(
        "mc,ck,cl->mkl",
        edges,
        projected,
        projected,
        precision=lax.Precision.HIGHEST,
        preferred_element_type=jnp.float32,
    )
    head_in, tail_in = halo(
        pack_symmetric(grams[0]),
        pack_symmetric(grams[1]),
        blk_index,
        blk_count,
        reach,
        edge_blocks,
        first_block,
        last_block,
    )
    head_in = unpack_symmetric(head_in)
    tail_in = unpack_symmetric(tail_in)
    own = (col_slot == my_slot).astype(jnp.float32)
    gram = jnp.einsum(
        "c,ck,cl->kl",
        own,
        projected,
        projected,
        precision=lax.Precision.HIGHEST,
        preferred_element_type=jnp.float32,
    )
    gram = lax.optimization_barrier(gram)
    gram = gram + jnp.where(my_slot == 0, head_in, 0.0)
    gram = gram + jnp.where(my_slot == last_slot, tail_in, 0.0)
    my_block = first_block + my_slot
    gram = gram / (block_units[my_block] * UNIT).astype(jnp.float32)
    return basis_rows(gram, my_rows)


def solution(mesh):
    return jax.shard_map(
        on_device,
        mesh=mesh,
        in_specs=(P("ind", "blk"), P(), P()),
        out_specs=P(("blk", "ind"), None),
        check_vma=False,
    )
```

```python
import jax
import jax.numpy as jnp
from jax import lax
from jax.sharding import PartitionSpec as P


K = 256
UNIT = 128
MAX_UNITS = 32
MIN_UNITS = 4

SHRINKAGE = 0.25


def sketch_signs(columns, seed_value, lane_count):
    lane_ids = jnp.arange(lane_count, dtype=jnp.int32)
    hashed = columns[:, None] * lane_count + lane_ids[None, :]
    hashed = jnp.bitwise_xor(hashed, seed_value)
    hashed = hashed * 73244475
    hashed = jnp.bitwise_xor(hashed, jnp.right_shift(hashed, 16))
    hashed = hashed * 73244475
    hashed = jnp.bitwise_xor(hashed, jnp.right_shift(hashed, 16))
    parity = jnp.bitwise_and(jnp.right_shift(hashed, 5), 1)
    return (1 - 2 * parity).astype(jnp.float32)


def xor_allreduce(x, axis, count):
    mask = 1
    while mask < count:
        x = x + lax.ppermute(x, axis, [(j, j ^ mask) for j in range(count)])
        mask *= 2
    return x


def ind_steps(count, place):
    if count % 2 or (count // 2) & (count // 2 - 1):
        steps = []
        mask = 1
        while mask < count:
            steps.append(([(j, j ^ mask) for j in range(count)], (place & mask) != 0))
            mask *= 2
        return steps
    rings = count // 2
    core = place % 2
    turned = (place // 2 + core) % rings
    steps = [([(j, j ^ 1) for j in range(count)], core != 0)]
    mask = 1
    while mask < rings:
        pairs = []
        for j in range(count):
            c, z = j % 2, j // 2
            partner = ((((z + c) % rings) ^ mask) - c) % rings
            pairs.append((j, partner * 2 + c))
        steps.append((pairs, (turned & mask) != 0))
        mask *= 2
    return steps


def halving_allreduce(x, axis, count, doubled_steps=1):
    steps = ind_steps(count, lax.axis_index(axis))
    split, doubled = steps[: len(steps) - doubled_steps], steps[len(steps) - doubled_steps :]
    for pairs, high in split:
        half = x.shape[0] // 2
        lower, upper = x[:half], x[half:]
        send = jnp.where(high, lower, upper)
        keep = jnp.where(high, upper, lower)
        x = keep + lax.ppermute(send, axis, pairs)
    for pairs, high in doubled:
        x = x + lax.ppermute(x, axis, pairs)
    for pairs, high in reversed(split):
        got = lax.ppermute(x, axis, pairs)
        x = jnp.where(high, jnp.concatenate([got, x], 0), jnp.concatenate([x, got], 0))
    return x


def dot_hi(a, b):
    return jnp.dot(a, b, precision=lax.Precision.HIGH, preferred_element_type=jnp.float32)


def lower_inverse(lower):
    eye = jnp.eye(lower.shape[0], dtype=lower.dtype)
    return jax.scipy.linalg.solve_triangular(lower, eye, lower=True)


def basis_rows(gram, rows):
    half = gram.shape[0] // 2
    l11 = jnp.linalg.cholesky(gram[:half, :half])
    m11 = lower_inverse(l11)
    l21 = dot_hi(gram[half:, :half], m11.T)
    l22 = jnp.linalg.cholesky(gram[half:, half:] - dot_hi(l21, l21.T))
    m22 = lower_inverse(l22)
    m21 = -dot_hi(m22, dot_hi(l21, m11))
    left = dot_hi(rows[:, :half], m11.T)
    right = dot_hi(rows[:, :half], m21.T) + dot_hi(rows[:, half:], m22.T)
    return jnp.concatenate([left, right], 1)


def pack_symmetric(gram):
    half = gram.shape[0] // 2
    corner = gram[half:, half:].reshape(half // 2, gram.shape[1])
    return jnp.concatenate([gram[:half], corner], 0)


def unpack_symmetric(packed):
    half = packed.shape[1] // 2
    top = packed[:half]
    corner = packed[half:].reshape(half, half)
    bottom = jnp.concatenate([top[:, half:].T, corner], 1)
    return jnp.concatenate([top, bottom], 0)


def shift(x, axis, count, step):
    pairs = [(j, j + step) for j in range(count) if 0 <= j + step < count]
    return lax.ppermute(x, axis, pairs)


def block_of(col, block_starts):
    return jnp.sum((col[..., None] >= block_starts).astype(jnp.int32), axis=-1) - 1


def halo(head_part, tail_part, blk_index, blk_count, reach, edge_blocks, first_block, last_block):
    head_part, tail_part = lax.optimization_barrier((head_part, tail_part))
    from_lower = []
    from_upper = []
    for step in range(1, reach + 1):
        got_tail = shift(tail_part, "blk", blk_count, step)
        got_head = shift(head_part, "blk", blk_count, -step)
        lower = blk_index - step
        upper = blk_index + step
        lower_ok = jnp.logical_and(
            lower >= 0, edge_blocks[jnp.clip(lower, 0, blk_count - 1), 1] == first_block
        )
        upper_ok = jnp.logical_and(
            upper < blk_count, edge_blocks[jnp.clip(upper, 0, blk_count - 1), 0] == last_block
        )
        from_lower.append(jnp.where(lower_ok, got_tail, 0.0))
        from_upper.append(jnp.where(upper_ok, got_head, 0.0))
    return sum(from_lower[1:], from_lower[0]), sum(from_upper[1:], from_upper[0])


def on_device(genotypes, block_units, sketch_seed):
    ind_count = lax.axis_size("ind")
    blk_count = lax.axis_size("blk")
    people, col_span = genotypes.shape
    everyone = people * ind_count
    row_slice = col_span // ind_count
    unit_count = col_span // UNIT
    slot_total = (unit_count - 1) // MIN_UNITS + 2
    reach = min(-(-(MAX_UNITS - 1) // unit_count), blk_count - 1)
    blk_index = lax.axis_index("blk")
    ind_index = lax.axis_index("ind")

    dosage = genotypes.astype(jnp.float32)
    stats = xor_allreduce(jnp.stack([jnp.sum(dosage, 0), jnp.sum(dosage * dosage, 0)]), "ind", ind_count)
    average = stats[0] / everyone
    spread_sq = stats[1] / everyone - average * average
    standard = ((dosage - average) * lax.rsqrt(spread_sq + 1e-05)).astype(jnp.bfloat16)

    widths = block_units * UNIT
    block_ends = jnp.cumsum(widths, dtype=jnp.int32)
    block_starts = block_ends - widths
    col_base = blk_index * col_span
    unit_cols = col_base + jnp.arange(unit_count, dtype=jnp.int32) * UNIT
    unit_block = block_of(unit_cols, block_starts)
    first_block = unit_block[0]
    last_block = unit_block[unit_count - 1]
    unit_slot = unit_block - first_block
    group_bases = jnp.arange(blk_count, dtype=jnp.int32) * col_span
    edge_blocks = jnp.stack(
        [block_of(group_bases, block_starts), block_of(group_bases + col_span - 1, block_starts)], 1
    )
    last_slot = last_block - first_block

    columns = col_base + jnp.arange(col_span, dtype=jnp.int32)
    signs = sketch_signs(columns, sketch_seed[0], K)
    signs_b = signs.astype(jnp.bfloat16)
    signs, signs_b = lax.optimization_barrier((signs, signs_b))
    slot_ids = jnp.arange(slot_total, dtype=jnp.int32)
    col_slot = jnp.repeat(unit_slot, UNIT)
    col_mask = col_slot[None, :] == slot_ids[:, None]
    masked_std = jnp.where(col_mask[:, None, :], standard[None], jnp.zeros((), jnp.bfloat16))

    parts = jnp.einsum(
        "snc,ck->snk", masked_std, signs_b, preferred_element_type=jnp.float32
    )
    head_in, tail_in = halo(
        parts[0], parts[last_slot], blk_index, blk_count, reach, edge_blocks, first_block, last_block
    )
    parts = parts.at[0].add(head_in)
    parts = parts.at[last_slot].add(tail_in)
    sketch = parts.astype(jnp.bfloat16)

    product = jnp.einsum("snc,snk->ck", masked_std, sketch, preferred_element_type=jnp.float32)
    product = halving_allreduce(product, "ind", ind_count)
    projected = product * ((1.0 - SHRINKAGE) / everyone) + SHRINKAGE * signs

    row_start = ind_index * row_slice
    my_rows = lax.dynamic_slice_in_dim(projected, row_start, row_slice, 0)
    my_slot = unit_slot[row_start // UNIT]
    edges = jnp.stack([col_slot == 0, col_slot == last_slot]).astype(jnp.float32)
    grams = jnp.einsum(
        "mc,ck,cl->mkl",
        edges,
        projected,
        projected,
        precision=lax.Precision.HIGH,
        preferred_element_type=jnp.float32,
    )
    head_in, tail_in = halo(
        pack_symmetric(grams[0]),
        pack_symmetric(grams[1]),
        blk_index,
        blk_count,
        reach,
        edge_blocks,
        first_block,
        last_block,
    )
    head_in = unpack_symmetric(head_in)
    tail_in = unpack_symmetric(tail_in)
    own = (col_slot == my_slot).astype(jnp.float32)
    gram = jnp.einsum(
        "c,ck,cl->kl",
        own,
        projected,
        projected,
        precision=lax.Precision.HIGH,
        preferred_element_type=jnp.float32,
    )
    gram = lax.optimization_barrier(gram)
    gram = gram + jnp.where(my_slot == 0, head_in, 0.0)
    gram = gram + jnp.where(my_slot == last_slot, tail_in, 0.0)
    my_block = first_block + my_slot
    gram = gram / (block_units[my_block] * UNIT).astype(jnp.float32)
    return basis_rows(gram, my_rows)


def solution(mesh):
    return jax.shard_map(
        on_device,
        mesh=mesh,
        in_specs=(P("ind", "blk"), P(), P()),
        out_specs=P(("blk", "ind"), None),
        check_vma=False,
    )
```
